256 devices in a mesh: rows: 8 (over y_hi, x), vecs: 32 (over y_lo, z, core).
Axes of the slice: x: 4, y: 4 (y_hi: 2, y_lo: 2; y = y_hi * 2 + y_lo), z: 8, core: 2. Of those that a mesh axis runs over, the one named last changes fastest.
Arguments:
- eigvecs: float32 [16384, 4096], P('rows', 'vecs'), may hold values from -6 to 6
- reflectors: float32 [7, 8192, 256], P(None, ('rows', 'vecs')), may hold values from -6 to 6
- offsets: int32 [7, 8], P(None, 'rows'), may hold values from 0 to 1024, as said below
Outputs:
- rotated: float32 [16384, 4096], P('rows', 'vecs')
The draws below stay inside these ranges and needn't reach their ends.
Inputs may be any that keep to these rules, and one draw needn't show every extreme that they name: `offsets`: in every tick some row block has offset 2048 - 1024 and another has offset 0.
All inputs are finite; a program needn't handle non-finite values.
Results may differ from the reference program's by a relative error of at most 0.00028.
Values sent between devices are 32-bit elements; how exact they have to be, the bound alone decides.
No kernel may reach another device: no remote copies, remote signals or barrier semaphores. Data moves between devices by JAX's collectives and lax.ppermute only.
A program may use at most 128 MiB of HBM per device.

```python
import jax
import jax.numpy as jnp
from jax import lax

NB = 1024
KB = 256
H = 256
R = 2048
TICKS = 7
GROUPS = 8
NROWS = 16384
NVEC = 4096


def draw_offsets(key, part):
    first_key, second_key = jax.random.split(jax.random.fold_in(key, 71))
    values = jax.random.randint(first_key, (TICKS, GROUPS), 0, R - NB + 1).astype(jnp.int32)
    chosen = jax.random.randint(second_key, (TICKS, 1), 0, GROUPS).astype(jnp.int32)
    columns = jnp.arange(GROUPS, dtype=jnp.int32)[None, :]
    values = jnp.where(columns == chosen, R - NB, values)
    values = jnp.where(columns == (chosen + 1) % GROUPS, 0, values)
    return values.astype(jnp.int32)


def block_levels(key, dims, cuts, least, top_value):
    def one(axis_at, parts):
        heights = jax.random.uniform(jax.random.fold_in(jax.random.fold_in(key, 6), axis_at), (parts,), jnp.float32, least / len(cuts), top_value / len(cuts))
        return jnp.repeat(jnp.exp(heights), dims[axis_at] // parts).reshape((-1,) + (1,) * (len(dims) - axis_at - 1))

    gain = one(*cuts[0])
    for cut in cuts[1:]:
        gain = gain * one(*cut)
    return gain


def scatter_about(stream_key, extent, deviation, limit, cuts=(), kind=jnp.bfloat16):
    array = deviation * jax.random.normal(stream_key, extent, jnp.float32)
    if cuts:
        array = array * block_levels(stream_key, extent, cuts, -0.22, 0.18)
    return jnp.clip(array, -limit, limit).astype(kind)


def setup_inputs(seed: int = 0) -> dict:
    seeds = jax.random.split(jax.random.key(seed), 4)
    eigvecs = scatter_about(seeds[0], (NROWS, NVEC), 1.0, 6.0, ((0, 8), (1, 32)), jnp.float32)
    reflectors = scatter_about(seeds[1], (TICKS, NB * GROUPS, KB), 1.0, 6.0, ((1, 256),), jnp.float32)
    offsets = draw_offsets(jax.random.fold_in(seeds[3], 71), 0)
    return dict(eigvecs=eigvecs, reflectors=reflectors, offsets=offsets)


def matmul_high(left, right):
    return jnp.dot(left, right, precision=lax.Precision.HIGHEST, preferred_element_type=jnp.float32)


def upper_inverse(tri):
    size = tri.shape[0]
    if size <= 32:
        diag_part = jnp.diagonal(tri)
        eye_part = jnp.eye(size, dtype=jnp.float32)
        nilpotent = tri / diag_part[:, None] - eye_part
        product = eye_part - nilpotent
        power = nilpotent
        span = 2
        while span < size:
            power = matmul_high(power, power)
            product = matmul_high(product, eye_part + power)
            span = span * 2
        return product * (1.0 / diag_part)[None, :]
    half = size // 2
    upper_inv = upper_inverse(tri[:half, :half])
    lower_inv = upper_inverse(tri[half:, half:])
    corner = -matmul_high(matmul_high(upper_inv, tri[:half, half:]), lower_inv)
    top = jnp.concatenate([upper_inv, corner], axis=1)
    bottom = jnp.concatenate([jnp.zeros((size - half, half), jnp.float32), lower_inv], axis=1)
    return jnp.concatenate([top, bottom], axis=0)


def apply_block(block, reflector, first_row):
    window = lax.dynamic_slice_in_dim(block, first_row, NB, 0)
    gram_matrix = matmul_high(reflector.T, reflector)
    inverse_t = jnp.triu(gram_matrix, 1) + jnp.diag(jnp.diagonal(gram_matrix)) * 0.5
    project = matmul_high(reflector.T, window)
    weights = matmul_high(upper_inverse(inverse_t), project)
    window = window - matmul_high(reflector, weights)
    return lax.dynamic_update_slice_in_dim(block, window, first_row, 0)


def apply_packed(operands):
    return apply_block(operands[0], operands[1], operands[2])


def reference(eigvecs, reflectors, offsets):
    blocks = eigvecs.reshape(GROUPS, R, eigvecs.shape[1])
    reflect_all = reflectors.reshape(TICKS, GROUPS, NB, KB)
    for step_index in range(TICKS):
        incoming = jnp.roll(blocks[:, R - H:], 1, axis=0)
        blocks = jnp.concatenate([incoming, blocks[:, :R - H]], axis=1)
        blocks = lax.map(apply_packed, (blocks, reflect_all[step_index], offsets[step_index]))
    return blocks.reshape(GROUPS * R, eigvecs.shape[1])
```

```python
import jax
import jax.numpy as jnp
from jax import lax
from jax.experimental import pallas as pl
from jax.sharding import PartitionSpec as P

NB = 1024
H = 256
TICKS = 7
BASE = 32


def passed_along(x, axis, by):
    size = lax.axis_size(axis)
    return lax.ppermute(x, axis, [(i, (i + by) % size) for i in range(size)])


def matmul_high(left, right):
    return jnp.dot(left, right, precision=lax.Precision.HIGHEST, preferred_element_type=jnp.float32)


def tri_inverse_kernel(g_ref, o_ref):
    g = g_ref[...]
    size = g.shape[0]
    row = lax.broadcasted_iota(jnp.int32, (size, size), 0)
    col = lax.broadcasted_iota(jnp.int32, (size, size), 1)
    eye_mask = row == col
    eye = eye_mask.astype(jnp.float32)
    a = jnp.where(col > row, g, jnp.where(eye_mask, g * 0.5, 0.0))
    diag_col = jnp.sum(jnp.where(eye_mask, a, 0.0), axis=1, keepdims=True)
    diag_row = jnp.sum(jnp.where(eye_mask, a, 0.0), axis=0, keepdims=True)
    same_base = (row // BASE) == (col // BASE)
    nilpotent = jnp.where(same_base, a / diag_col, 0.0) - eye

    def square(_, carry):
        product, power = carry
        power = matmul_high(power, power)
        return matmul_high(product, eye + power), power

    product, _ = lax.fori_loop(0, BASE.bit_length() - 2, square, (eye - nilpotent, nilpotent))
    inv = product * (1.0 / diag_row)
    row_shift = jnp.right_shift(row, BASE.bit_length() - 1)
    col_shift = jnp.right_shift(col, BASE.bit_length() - 1)

    def merge(level, inv):
        row_blk = jnp.right_shift(row_shift, level)
        col_blk = jnp.right_shift(col_shift, level)
        corner_mask = (jnp.bitwise_and(row_blk, 1) == 0) & (col_blk == row_blk + 1)
        upper = jnp.where(corner_mask, a, 0.0)
        return inv - matmul_high(matmul_high(inv, upper), inv)

    inv = lax.fori_loop(0, size.bit_length() - BASE.bit_length(), merge, inv)
    o_ref[...] = inv


def tri_inverse(gram):
    return pl.pallas_call(
        tri_inverse_kernel,
        out_shape=jax.ShapeDtypeStruct(gram.shape, jnp.float32),
    )(gram)


def shards(eigvecs, reflectors, offsets):
    rows_here = eigvecs.shape[0]
    kb = reflectors.shape[-1]
    block = eigvecs
    outgoing = block[rows_here - H :]
    for step_index in range(TICKS):
        reflector = lax.all_gather(reflectors[step_index], "vecs", axis=0, tiled=True)
        gram = lax.dot_general(
            reflector, reflector, (((0,), (0,)), ((), ())),
            precision=lax.Precision.HIGHEST, preferred_element_type=jnp.float32,
        )
        solve = tri_inverse(gram)
        placed = lax.dynamic_update_slice_in_dim(
            jnp.zeros((rows_here, kb), jnp.float32), reflector, offsets[step_index, 0], 0
        )
        own = block[: rows_here - H]
        incoming = passed_along(outgoing, "rows", 1)
        project = lax.dot_general(
            placed[H:], own, (((0,), (0,)), ((), ())),
            precision=lax.Precision.HIGHEST, preferred_element_type=jnp.float32,
        ) + lax.dot_general(
            placed[:H], incoming, (((0,), (0,)), ((), ())),
            precision=lax.Precision.HIGHEST, preferred_element_type=jnp.float32,
        )
        weights = matmul_high(solve, project)
        block = jnp.concatenate([incoming, own], axis=0)
        if step_index + 1 < TICKS:
            outgoing = block[rows_here - H :] - matmul_high(placed[rows_here - H :], weights)
        block = block - matmul_high(placed, weights)
    return block


def solution(mesh):
    in_specs = (P("rows", "vecs"), P(None, ("rows", "vecs"), None), P(None, "rows"))
    out_specs = P("rows", "vecs")
    return jax.shard_map(shards, mesh=mesh, in_specs=in_specs, out_specs=out_specs, check_vma=False)
```

```python
import jax
import jax.numpy as jnp
from jax import lax
from jax.sharding import PartitionSpec as P

H = 256
TICKS = 7
BASE = 32


def passed_along(x, axis, by):
    size = lax.axis_size(axis)
    return lax.ppermute(x, axis, [(i, (i + by) % size) for i in range(size)])


def matmul_high(left, right):
    return jnp.matmul(left, right, precision=lax.Precision.HIGHEST, preferred_element_type=jnp.float32)


def project_onto(left, right):
    return lax.dot_general(
        left, right, (((left.ndim - 2,), (right.ndim - 2,)), ((), ())),
        precision=lax.Precision.HIGHEST, preferred_element_type=jnp.float32,
    )


def tri_inverses(gram):
    size = gram.shape[-1]
    row = lax.broadcasted_iota(jnp.int32, (size, size), 0)
    col = lax.broadcasted_iota(jnp.int32, (size, size), 1)
    eye_mask = row == col
    eye = eye_mask.astype(jnp.float32)
    a = jnp.where(col > row, gram, jnp.where(eye_mask, gram * 0.5, 0.0))
    diag_part = jnp.sum(jnp.where(eye_mask, a, 0.0), axis=-1)
    same_base = (row // BASE) == (col // BASE)
    nilpotent = jnp.where(same_base, a / diag_part[..., :, None], 0.0) - eye
    product = eye - nilpotent
    power = nilpotent
    span = 2
    while span < BASE:
        power = matmul_high(power, power)
        product = matmul_high(product, eye + power)
        span = span * 2
    inv = product * (1.0 / diag_part)[..., None, :]
    half = BASE
    while half < size:
        corner_mask = ((row // half) % 2 == 0) & ((col // half) == (row // half) + 1)
        upper = jnp.where(corner_mask, a, 0.0)
        inv = inv - matmul_high(matmul_high(inv, upper), inv)
        half = half * 2
    return inv


def placed_reflectors(reflectors, offsets, rows_here):
    nb = reflectors.shape[1]
    index = jnp.arange(rows_here, dtype=jnp.int32)[None, :] - offsets[:, None]
    inside = (index >= 0) & (index < nb)
    taken = jnp.take_along_axis(reflectors, jnp.clip(index, 0, nb - 1)[:, :, None], axis=1)
    return jnp.where(inside[:, :, None], taken, 0.0)


def shards(eigvecs, reflectors, offsets):
    rows_here = eigvecs.shape[0]
    gathered = lax.all_gather(reflectors, "vecs", axis=1, tiled=True)
    gram = jnp.einsum("tkr,tks->trs", gathered, gathered, precision=lax.Precision.HIGHEST, preferred_element_type=jnp.float32)
    solves = tri_inverses(gram)
    placed_all = placed_reflectors(gathered, offsets[:, 0], rows_here)
    block = eigvecs
    outgoing = block[rows_here - H :]
    for step_index in range(TICKS):
        placed = placed_all[step_index]
        own = block[: rows_here - H]
        incoming = passed_along(outgoing, "rows", 1)
        project = project_onto(placed[H:], own) + project_onto(placed[:H], incoming)
        weights = matmul_high(solves[step_index], project)
        block = jnp.concatenate([incoming, own], axis=0)
        if step_index + 1 < TICKS:
            outgoing = block[rows_here - H :] - matmul_high(placed[rows_here - H :], weights)
        block = block - matmul_high(placed, weights)
    return block


def solution(mesh):
    in_specs = (P("rows", "vecs"), P(None, ("rows", "vecs"), None), P(None, "rows"))
    out_specs = P("rows", "vecs")
    return jax.shard_map(shards, mesh=mesh, in_specs=in_specs, out_specs=out_specs, check_vma=False)
```

```python
import jax
import jax.numpy as jnp
from jax import lax
from jax.experimental import pallas as pl
from jax.sharding import PartitionSpec as P

H = 256
TICKS = 7
BASE = 32


def passed_along(x, axis, by):
    size = lax.axis_size(axis)
    return lax.ppermute(x, axis, [(i, (i + by) % size) for i in range(size)])


def matmul_high(left, right):
    return jnp.matmul(left, right, precision=lax.Precision.HIGHEST, preferred_element_type=jnp.float32)


def project_onto(left, right):
    return lax.dot_general(
        left, right, (((left.ndim - 2,), (right.ndim - 2,)), ((), ())),
        precision=lax.Precision.HIGHEST, preferred_element_type=jnp.float32,
    )


def half_inverse(a, size):
    row = lax.broadcasted_iota(jnp.int32, (size, size), 0)
    col = lax.broadcasted_iota(jnp.int32, (size, size), 1)
    eye_mask = row == col
    eye = eye_mask.astype(jnp.float32)
    diag_col = jnp.sum(jnp.where(eye_mask, a, 0.0), axis=1, keepdims=True)
    diag_row = jnp.sum(jnp.where(eye_mask, a, 0.0), axis=0, keepdims=True)
    same_base = (row // BASE) == (col // BASE)
    nilpotent = jnp.where(same_base, a / diag_col, 0.0) - eye
    product = eye - nilpotent
    power = nilpotent
    span = 2
    while span < BASE:
        power = matmul_high(power, power)
        product = matmul_high(product, eye + power)
        span = span * 2
    inv = product * (1.0 / diag_row)
    half = BASE
    while half < size:
        corner_mask = ((row // half) % 2 == 0) & ((col // half) == (row // half) + 1)
        upper = jnp.where(corner_mask, a, 0.0)
        inv = inv - matmul_high(matmul_high(inv, upper), inv)
        half = half * 2
    return inv


def tri_inverse_kernel(g_ref, o_ref):
    size = g_ref.shape[0]
    half = size // 2
    row = lax.broadcasted_iota(jnp.int32, (half, half), 0)
    col = lax.broadcasted_iota(jnp.int32, (half, half), 1)

    def upper_part(x):
        return jnp.where(col > row, x, jnp.where(row == col, x * 0.5, 0.0))

    upper_inv = half_inverse(upper_part(g_ref[:half, :half]), half)
    lower_inv = half_inverse(upper_part(g_ref[half:, half:]), half)
    corner = -matmul_high(matmul_high(upper_inv, g_ref[:half, half:]), lower_inv)
    o_ref[:half, :half] = upper_inv
    o_ref[:half, half:] = corner
    o_ref[half:, :half] = jnp.zeros((half, half), jnp.float32)
    o_ref[half:, half:] = lower_inv


def tri_inverse(gram):
    return pl.pallas_call(
        tri_inverse_kernel,
        out_shape=jax.ShapeDtypeStruct(gram.shape, jnp.float32),
    )(gram)


def placed_reflector(reflector, first_row, rows_here):
    nb = reflector.shape[0]
    padded = jnp.pad(reflector, ((rows_here - nb, rows_here - nb), (0, 0)))
    return lax.dynamic_slice_in_dim(padded, rows_here - nb - first_row, rows_here, 0)


def shards(eigvecs, reflectors, offsets):
    rows_here = eigvecs.shape[0]
    gathered = lax.all_gather(reflectors, "vecs", axis=1, tiled=True)
    block = eigvecs
    outgoing = block[rows_here - H :]
    for step_index in range(TICKS):
        reflector = gathered[step_index]
        solve = tri_inverse(project_onto(reflector, reflector))
        placed = placed_reflector(reflector, offsets[step_index, 0], rows_here)
        own = block[: rows_here - H]
        incoming = passed_along(outgoing, "rows", 1)
        project = project_onto(placed[H:], own) + project_onto(placed[:H], incoming)
        weights = matmul_high(solve, project)
        block = jnp.concatenate([incoming, own], axis=0)
        if step_index + 1 < TICKS:
            outgoing = block[rows_here - H :] - matmul_high(placed[rows_here - H :], weights)
        block = block - matmul_high(placed, weights)
    return block


def solution(mesh):
    in_specs = (P("rows", "vecs"), P(None, ("rows", "vecs"), None), P(None, "rows"))
    out_specs = P("rows", "vecs")
    return jax.shard_map(shards, mesh=mesh, in_specs=in_specs, out_specs=out_specs, check_vma=False)
```

```python
import jax
import jax.numpy as jnp
from jax import lax
from jax.experimental import pallas as pl
from jax.sharding import PartitionSpec as P

H = 256
BASE = 32


def passed_along(x, axis, by):
    size = lax.axis_size(axis)
    return lax.ppermute(x, axis, [(i, (i + by) % size) for i in range(size)])


def matmul_high(left, right):
    return jnp.matmul(left, right, precision=lax.Precision.HIGHEST, preferred_element_type=jnp.float32)


def project_onto(left, right):
    return lax.dot_general(
        left, right, (((left.ndim - 2,), (right.ndim - 2,)), ((), ())),
        precision=lax.Precision.HIGHEST, preferred_element_type=jnp.float32,
    )


def half_inverse(a, size):
    row = lax.broadcasted_iota(jnp.int32, (size, size), 0)
    col = lax.broadcasted_iota(jnp.int32, (size, size), 1)
    eye_mask = row == col
    eye = eye_mask.astype(jnp.float32)
    diag_col = jnp.sum(jnp.where(eye_mask, a, 0.0), axis=1, keepdims=True)
    diag_row = jnp.sum(jnp.where(eye_mask, a, 0.0), axis=0, keepdims=True)
    same_base = (row // BASE) == (col // BASE)
    nilpotent = jnp.where(same_base, a / diag_col, 0.0) - eye
    product = eye - nilpotent
    power = nilpotent
    span = 2
    while span < BASE:
        power = matmul_high(power, power)
        product = matmul_high(product, eye + power)
        span = span * 2
    inv = product * (1.0 / diag_row)
    half = BASE
    while half < size:
        corner_mask = ((row // half) % 2 == 0) & ((col // half) == (row // half) + 1)
        upper = jnp.where(corner_mask, a, 0.0)
        inv = inv - matmul_high(matmul_high(inv, upper), inv)
        half = half * 2
    return inv


def tri_inverse_kernel(g_ref, o_ref):
    size = g_ref.shape[0]
    half = size // 2
    row = lax.broadcasted_iota(jnp.int32, (half, half), 0)
    col = lax.broadcasted_iota(jnp.int32, (half, half), 1)

    def upper_part(x):
        return jnp.where(col > row, x, jnp.where(row == col, x * 0.5, 0.0))

    upper_inv = half_inverse(upper_part(g_ref[:half, :half]), half)
    lower_inv = half_inverse(upper_part(g_ref[half:, half:]), half)
    corner = -matmul_high(matmul_high(upper_inv, g_ref[:half, half:]), lower_inv)
    o_ref[:half, :half] = upper_inv
    o_ref[:half, half:] = corner
    o_ref[half:, :half] = jnp.zeros((half, half), jnp.float32)
    o_ref[half:, half:] = lower_inv


def tri_inverse(gram):
    return pl.pallas_call(
        tri_inverse_kernel,
        out_shape=jax.ShapeDtypeStruct(gram.shape, jnp.float32),
    )(gram)


def placed_reflector(reflector, first_row, rows_here):
    nb = reflector.shape[0]
    padded = jnp.pad(reflector, ((rows_here - nb, rows_here - nb), (0, 0)))
    return lax.dynamic_slice_in_dim(padded, rows_here - nb - first_row, rows_here, 0)


def shards(eigvecs, reflectors, offsets):
    rows_here = eigvecs.shape[0]
    ticks = reflectors.shape[0]
    gathered = lax.all_gather(reflectors, "vecs", axis=1, tiled=True)
    first_rows = offsets[:, 0]

    def prepare(step, block):
        reflector = lax.dynamic_index_in_dim(gathered, step, 0, keepdims=False)
        solve = tri_inverse(project_onto(reflector, reflector))
        placed = placed_reflector(reflector, first_rows[step], rows_here)
        own_part = lax.optimization_barrier(project_onto(placed[H:], block[: rows_here - H]))
        return placed, own_part, solve

    def finish(block, incoming, placed, own_part, solve):
        project = own_part + project_onto(placed[:H], incoming)
        weights = matmul_high(solve, project)
        return weights, jnp.concatenate([incoming, block[: rows_here - H]], axis=0)

    def tick(step, carry):
        block, incoming, placed, own_part, solve = carry
        weights, joined = finish(block, incoming, placed, own_part, solve)
        outgoing = block[rows_here - 2 * H : rows_here - H] - matmul_high(placed[rows_here - H :], weights)
        incoming = passed_along(outgoing, "rows", 1)
        block = joined - matmul_high(placed, weights)
        return (block, incoming) + prepare(step + 1, block)

    carry = (eigvecs, passed_along(eigvecs[rows_here - H :], "rows", 1)) + prepare(0, eigvecs)
    carry = lax.fori_loop(0, ticks - 1, tick, carry)
    block, incoming, placed, own_part, solve = carry
    weights, joined = finish(block, incoming, placed, own_part, solve)
    return joined - matmul_high(placed, weights)


def solution(mesh):
    in_specs = (P("rows", "vecs"), P(None, ("rows", "vecs"), None), P(None, "rows"))
    out_specs = P("rows", "vecs")
    return jax.shard_map(shards, mesh=mesh, in_specs=in_specs, out_specs=out_specs, check_vma=False)
```

```python
import jax
import jax.numpy as jnp
from jax import lax
from jax.experimental import pallas as pl
from jax.sharding import PartitionSpec as P

H = 256
BASE = 32


def passed_along(x, axis, by):
    size = lax.axis_size(axis)
    return lax.ppermute(x, axis, [(i, (i + by) % size) for i in range(size)])


def matmul_high(left, right):
    return jnp.matmul(left, right, precision=lax.Precision.HIGHEST, preferred_element_type=jnp.float32)


def matmul_3x(left, right):
    return jnp.matmul(left, right, precision=lax.Precision.HIGH, preferred_element_type=jnp.float32)


def project_onto(left, right):
    return lax.dot_general(
        left, right, (((left.ndim - 2,), (right.ndim - 2,)), ((), ())),
        precision=lax.Precision.HIGH, preferred_element_type=jnp.float32,
    )


def half_inverse(a, size):
    row = lax.broadcasted_iota(jnp.int32, (size, size), 0)
    col = lax.broadcasted_iota(jnp.int32, (size, size), 1)
    eye_mask = row == col
    eye = eye_mask.astype(jnp.float32)
    diag_col = jnp.sum(jnp.where(eye_mask, a, 0.0), axis=1, keepdims=True)
    diag_row = jnp.sum(jnp.where(eye_mask, a, 0.0), axis=0, keepdims=True)
    same_base = (row // BASE) == (col // BASE)
    nilpotent = jnp.where(same_base, a / diag_col, 0.0) - eye
    product = eye - nilpotent
    power = nilpotent
    span = 2
    while span < BASE:
        power = matmul_high(power, power)
        product = matmul_high(product, eye + power)
        span = span * 2
    inv = product * (1.0 / diag_row)
    half = BASE
    while half < size:
        corner_mask = ((row // half) % 2 == 0) & ((col // half) == (row // half) + 1)
        upper = jnp.where(corner_mask, a, 0.0)
        inv = inv - matmul_high(matmul_high(inv, upper), inv)
        half = half * 2
    return inv


def tri_inverse_kernel(g_ref, o_ref):
    size = g_ref.shape[0]
    half = size // 2
    row = lax.broadcasted_iota(jnp.int32, (half, half), 0)
    col = lax.broadcasted_iota(jnp.int32, (half, half), 1)

    def upper_part(x):
        return jnp.where(col > row, x, jnp.where(row == col, x * 0.5, 0.0))

    upper_inv = half_inverse(upper_part(g_ref[:half, :half]), half)
    lower_inv = half_inverse(upper_part(g_ref[half:, half:]), half)
    corner = -matmul_high(matmul_high(upper_inv, g_ref[:half, half:]), lower_inv)
    o_ref[:half, :half] = upper_inv
    o_ref[:half, half:] = corner
    o_ref[half:, :half] = jnp.zeros((half, half), jnp.float32)
    o_ref[half:, half:] = lower_inv


def tri_inverse(gram):
    return pl.pallas_call(
        tri_inverse_kernel,
        out_shape=jax.ShapeDtypeStruct(gram.shape, jnp.float32),
    )(gram)


def placed_reflector(reflector, first_row, rows_here):
    nb = reflector.shape[0]
    padded = jnp.pad(reflector, ((rows_here - nb, rows_here - nb), (0, 0)))
    return lax.dynamic_slice_in_dim(padded, rows_here - nb - first_row, rows_here, 0)


def shards(eigvecs, reflectors, offsets):
    rows_here = eigvecs.shape[0]
    ticks = reflectors.shape[0]
    gathered = lax.all_gather(reflectors, "vecs", axis=1, tiled=True)
    first_rows = offsets[:, 0]

    def prepare(step, block):
        reflector = lax.dynamic_index_in_dim(gathered, step, 0, keepdims=False)
        solve = tri_inverse(project_onto(reflector, reflector))
        placed = placed_reflector(reflector, first_rows[step], rows_here)
        own_part = lax.optimization_barrier(project_onto(placed[H:], block[: rows_here - H]))
        return placed, own_part, solve

    def finish(block, incoming, placed, own_part, solve):
        project = own_part + project_onto(placed[:H], incoming)
        weights = matmul_3x(solve, project)
        return weights, jnp.concatenate([incoming, block[: rows_here - H]], axis=0)

    def tick(step, carry):
        block, incoming, placed, own_part, solve = carry
        weights, joined = finish(block, incoming, placed, own_part, solve)
        outgoing = block[rows_here - 2 * H : rows_here - H] - matmul_3x(placed[rows_here - H :], weights)
        incoming = passed_along(outgoing, "rows", 1)
        block = joined - matmul_3x(placed, weights)
        return (block, incoming) + prepare(step + 1, block)

    carry = (eigvecs, passed_along(eigvecs[rows_here - H :], "rows", 1)) + prepare(0, eigvecs)
    carry = lax.fori_loop(0, ticks - 1, tick, carry)
    block, incoming, placed, own_part, solve = carry
    weights, joined = finish(block, incoming, placed, own_part, solve)
    return joined - matmul_3x(placed, weights)


def solution(mesh):
    in_specs = (P("rows", "vecs"), P(None, ("rows", "vecs"), None), P(None, "rows"))
    out_specs = P("rows", "vecs")
    return jax.shard_map(shards, mesh=mesh, in_specs=in_specs, out_specs=out_specs, check_vma=False)
```

```python
import jax
import jax.numpy as jnp
from jax import lax
from jax.experimental import pallas as pl
from jax.sharding import PartitionSpec as P

H = 256
BASE = 32


def passed_along(x, axis, by):
    size = lax.axis_size(axis)
    return lax.ppermute(x, axis, [(i, (i + by) % size) for i in range(size)])


def matmul_3x(left, right):
    return jnp.matmul(left, right, precision=lax.Precision.HIGH, preferred_element_type=jnp.float32)


def project_onto(left, right):
    return lax.dot_general(
        left, right, (((left.ndim - 2,), (right.ndim - 2,)), ((), ())),
        precision=lax.Precision.HIGH, preferred_element_type=jnp.float32,
    )


def half_inverse(a, size):
    row = lax.broadcasted_iota(jnp.int32, (size, size), 0)
    col = lax.broadcasted_iota(jnp.int32, (size, size), 1)
    eye_mask = row == col
    eye = eye_mask.astype(jnp.float32)
    diag_col = jnp.sum(jnp.where(eye_mask, a, 0.0), axis=1, keepdims=True)
    diag_row = jnp.sum(jnp.where(eye_mask, a, 0.0), axis=0, keepdims=True)
    same_base = (row // BASE) == (col // BASE)
    nilpotent = jnp.where(same_base, a / diag_col, 0.0) - eye
    product = eye - nilpotent
    power = nilpotent
    span = 2
    while span < BASE:
        power = matmul_3x(power, power)
        product = matmul_3x(product, eye + power)
        span = span * 2
    inv = product * (1.0 / diag_row)
    half = BASE
    while half < size:
        corner_mask = ((row // half) % 2 == 0) & ((col // half) == (row // half) + 1)
        upper = jnp.where(corner_mask, a, 0.0)
        inv = inv - matmul_3x(matmul_3x(inv, upper), inv)
        half = half * 2
    return inv


def tri_inverse_kernel(g_ref, o_ref):
    size = g_ref.shape[0]
    half = size // 2
    row = lax.broadcasted_iota(jnp.int32, (half, half), 0)
    col = lax.broadcasted_iota(jnp.int32, (half, half), 1)

    def upper_part(x):
        return jnp.where(col > row, x, jnp.where(row == col, x * 0.5, 0.0))

    upper_inv = half_inverse(upper_part(g_ref[:half, :half]), half)
    lower_inv = half_inverse(upper_part(g_ref[half:, half:]), half)
    corner = -matmul_3x(matmul_3x(upper_inv, g_ref[:half, half:]), lower_inv)
    o_ref[:half, :half] = upper_inv
    o_ref[:half, half:] = corner
    o_ref[half:, :half] = jnp.zeros((half, half), jnp.float32)
    o_ref[half:, half:] = lower_inv


def tri_inverse(gram):
    return pl.pallas_call(
        tri_inverse_kernel,
        out_shape=jax.ShapeDtypeStruct(gram.shape, jnp.float32),
    )(gram)


def placed_reflector(reflector, first_row, rows_here):
    nb = reflector.shape[0]
    padded = jnp.pad(reflector, ((rows_here - nb, rows_here - nb), (0, 0)))
    return lax.dynamic_slice_in_dim(padded, rows_here - nb - first_row, rows_here, 0)


def shards(eigvecs, reflectors, offsets):
    rows_here = eigvecs.shape[0]
    ticks = reflectors.shape[0]
    gathered = lax.all_gather(reflectors, "vecs", axis=1, tiled=True)
    first_rows = offsets[:, 0]

    def prepare(step, block):
        reflector = lax.dynamic_index_in_dim(gathered, step, 0, keepdims=False)
        solve = tri_inverse(project_onto(reflector, reflector))
        placed = placed_reflector(reflector, first_rows[step], rows_here)
        own_part = lax.optimization_barrier(project_onto(placed[H:], block[: rows_here - H]))
        return placed, own_part, solve

    def finish(block, incoming, placed, own_part, solve):
        project = own_part + project_onto(placed[:H], incoming)
        weights = matmul_3x(solve, project)
        return weights, jnp.concatenate([incoming, block[: rows_here - H]], axis=0)

    def tick(step, carry):
        block, incoming, placed, own_part, solve = carry
        weights, joined = finish(block, incoming, placed, own_part, solve)
        outgoing = block[rows_here - 2 * H : rows_here - H] - matmul_3x(placed[rows_here - H :], weights)
        incoming = passed_along(outgoing, "rows", 1)
        block = joined - matmul_3x(placed, weights)
        return (block, incoming) + prepare(step + 1, block)

    carry = (eigvecs, passed_along(eigvecs[rows_here - H :], "rows", 1)) + prepare(0, eigvecs)
    carry = lax.fori_loop(0, ticks - 1, tick, carry)
    block, incoming, placed, own_part, solve = carry
    weights, joined = finish(block, incoming, placed, own_part, solve)
    return joined - matmul_3x(placed, weights)


def solution(mesh):
    in_specs = (P("rows", "vecs"), P(None, ("rows", "vecs"), None), P(None, "rows"))
    out_specs = P("rows", "vecs")
    return jax.shard_map(shards, mesh=mesh, in_specs=in_specs, out_specs=out_specs, check_vma=False)
```

```python
import jax
import jax.numpy as jnp
from jax import lax
from jax.experimental import pallas as pl
from jax.sharding import PartitionSpec as P

H = 256
BASE = 32


def passed_along(x, axis, by):
    size = lax.axis_size(axis)
    return lax.ppermute(x, axis, [(i, (i + by) % size) for i in range(size)])


def matmul_3x(left, right):
    return jnp.matmul(left, right, precision=lax.Precision.HIGH, preferred_element_type=jnp.float32)


def project_onto(left, right):
    return lax.dot_general(
        left, right, (((left.ndim - 2,), (right.ndim - 2,)), ((), ())),
        precision=lax.Precision.HIGH, preferred_element_type=jnp.float32,
    )


def half_inverses(blocks, size):
    row = lax.broadcasted_iota(jnp.int32, (size, size), 0)
    col = lax.broadcasted_iota(jnp.int32, (size, size), 1)
    eye_mask = row == col
    eye = eye_mask.astype(jnp.float32)
    same_base = (row // BASE) == (col // BASE)
    diag_cols = [jnp.sum(jnp.where(eye_mask, a, 0.0), axis=1, keepdims=True) for a in blocks]
    diag_rows = [jnp.sum(jnp.where(eye_mask, a, 0.0), axis=0, keepdims=True) for a in blocks]
    powers = [jnp.where(same_base, a / d, 0.0) - eye for a, d in zip(blocks, diag_cols)]
    products = [eye - p for p in powers]
    span = 2
    while span < BASE:
        powers = [matmul_3x(p, p) for p in powers]
        products = [matmul_3x(q, eye + p) for q, p in zip(products, powers)]
        span = span * 2
    invs = [q * (1.0 / d) for q, d in zip(products, diag_rows)]
    half = BASE
    while half < size:
        corner_mask = ((row // half) % 2 == 0) & ((col // half) == (row // half) + 1)
        uppers = [jnp.where(corner_mask, a, 0.0) for a in blocks]
        invs = [v - matmul_3x(matmul_3x(v, u), v) for v, u in zip(invs, uppers)]
        half = half * 2
    return invs


def tri_inverse_kernel(g_ref, o_ref):
    ticks, size = g_ref.shape[0], g_ref.shape[1]
    half = size // 2
    row = lax.broadcasted_iota(jnp.int32, (half, half), 0)
    col = lax.broadcasted_iota(jnp.int32, (half, half), 1)

    def upper_part(x):
        return jnp.where(col > row, x, jnp.where(row == col, x * 0.5, 0.0))

    blocks = []
    for t in range(ticks):
        blocks.append(upper_part(g_ref[t, :half, :half]))
        blocks.append(upper_part(g_ref[t, half:, half:]))
    invs = half_inverses(blocks, half)
    for t in range(ticks):
        upper_inv, lower_inv = invs[2 * t], invs[2 * t + 1]
        corner = -matmul_3x(matmul_3x(upper_inv, g_ref[t, :half, half:]), lower_inv)
        o_ref[t, :half, :half] = upper_inv
        o_ref[t, :half, half:] = corner
        o_ref[t, half:, :half] = jnp.zeros((half, half), jnp.float32)
        o_ref[t, half:, half:] = lower_inv


def tri_inverse(gram):
    return pl.pallas_call(
        tri_inverse_kernel,
        out_shape=jax.ShapeDtypeStruct(gram.shape, jnp.float32),
    )(gram)


def placed_reflector(reflector, first_row, rows_here):
    nb = reflector.shape[0]
    padded = jnp.pad(reflector, ((rows_here - nb, rows_here - nb), (0, 0)))
    return lax.dynamic_slice_in_dim(padded, rows_here - nb - first_row, rows_here, 0)


def shards(eigvecs, reflectors, offsets):
    rows_here = eigvecs.shape[0]
    ticks = reflectors.shape[0]
    gathered = lax.all_gather(reflectors, "vecs", axis=1, tiled=True)
    grams = jnp.einsum("tkr,tks->trs", gathered, gathered, precision=lax.Precision.HIGH, preferred_element_type=jnp.float32)
    solves = tri_inverse(grams)
    first_rows = offsets[:, 0]

    def prepare(step, block):
        reflector = lax.dynamic_index_in_dim(gathered, step, 0, keepdims=False)
        solve = lax.dynamic_index_in_dim(solves, step, 0, keepdims=False)
        placed = placed_reflector(reflector, first_rows[step], rows_here)
        own_part = lax.optimization_barrier(project_onto(placed[H:], block[: rows_here - H]))
        return placed, own_part, solve

    def finish(block, incoming, placed, own_part, solve):
        project = own_part + project_onto(placed[:H], incoming)
        weights = matmul_3x(solve, project)
        return weights, jnp.concatenate([incoming, block[: rows_here - H]], axis=0)

    def tick(step, carry):
        block, incoming, placed, own_part, solve = carry
        weights, joined = finish(block, incoming, placed, own_part, solve)
        outgoing = block[rows_here - 2 * H : rows_here - H] - matmul_3x(placed[rows_here - H :], weights)
        incoming = passed_along(outgoing, "rows", 1)
        block = joined - matmul_3x(placed, weights)
        return (block, incoming) + prepare(step + 1, block)

    carry = (eigvecs, passed_along(eigvecs[rows_here - H :], "rows", 1)) + prepare(0, eigvecs)
    carry = lax.fori_loop(0, ticks - 1, tick, carry)
    block, incoming, placed, own_part, solve = carry
    weights, joined = finish(block, incoming, placed, own_part, solve)
    return joined - matmul_3x(placed, weights)


def solution(mesh):
    in_specs = (P("rows", "vecs"), P(None, ("rows", "vecs"), None), P(None, "rows"))
    out_specs = P("rows", "vecs")
    return jax.shard_map(shards, mesh=mesh, in_specs=in_specs, out_specs=out_specs, check_vma=False)
```

```python
import jax
import jax.numpy as jnp
from jax import lax
from jax.experimental import pallas as pl
from jax.sharding import PartitionSpec as P

H = 256
BASE = 32


def passed_along(x, axis, by):
    size = lax.axis_size(axis)
    return lax.ppermute(x, axis, [(i, (i + by) % size) for i in range(size)])


def matmul_3x(left, right):
    return jnp.matmul(left, right, precision=lax.Precision.HIGH, preferred_element_type=jnp.float32)


def project_onto(left, right):
    return lax.dot_general(
        left, right, (((left.ndim - 2,), (right.ndim - 2,)), ((), ())),
        precision=lax.Precision.HIGH, preferred_element_type=jnp.float32,
    )


def half_inverses(blocks, size):
    row = lax.broadcasted_iota(jnp.int32, (size, size), 0)
    col = lax.broadcasted_iota(jnp.int32, (size, size), 1)
    eye_mask = row == col
    eye = eye_mask.astype(jnp.float32)
    same_base = (row // BASE) == (col // BASE)
    diag_cols = [jnp.sum(jnp.where(eye_mask, a, 0.0), axis=1, keepdims=True) for a in blocks]
    diag_rows = [jnp.sum(jnp.where(eye_mask, a, 0.0), axis=0, keepdims=True) for a in blocks]
    powers = [jnp.where(same_base, a / d, 0.0) - eye for a, d in zip(blocks, diag_cols)]
    products = [eye - p for p in powers]
    span = 2
    while span < BASE:
        powers = [matmul_3x(p, p) for p in powers]
        products = [matmul_3x(q, eye + p) for q, p in zip(products, powers)]
        span = span * 2
    invs = [q * (1.0 / d) for q, d in zip(products, diag_rows)]
    half = BASE
    while half < size:
        corner_mask = ((row // half) % 2 == 0) & ((col // half) == (row // half) + 1)
        uppers = [jnp.where(corner_mask, a, 0.0) for a in blocks]
        invs = [v - matmul_3x(matmul_3x(v, u), v) for v, u in zip(invs, uppers)]
        half = half * 2
    return invs


def tri_inverse_kernel(g_ref, o_ref):
    ticks, size = g_ref.shape[0], g_ref.shape[1]
    half = size // 2
    row = lax.broadcasted_iota(jnp.int32, (half, half), 0)
    col = lax.broadcasted_iota(jnp.int32, (half, half), 1)

    def upper_part(x):
        return jnp.where(col > row, x, jnp.where(row == col, x * 0.5, 0.0))

    blocks = []
    for t in range(ticks):
        blocks.append(upper_part(g_ref[t, :half, :half]))
        blocks.append(upper_part(g_ref[t, half:, half:]))
    invs = half_inverses(blocks, half)
    for t in range(ticks):
        upper_inv, lower_inv = invs[2 * t], invs[2 * t + 1]
        corner = -matmul_3x(matmul_3x(upper_inv, g_ref[t, :half, half:]), lower_inv)
        o_ref[t, :half, :half] = upper_inv
        o_ref[t, :half, half:] = corner
        o_ref[t, half:, :half] = jnp.zeros((half, half), jnp.float32)
        o_ref[t, half:, half:] = lower_inv


def tri_inverse(gram):
    return pl.pallas_call(
        tri_inverse_kernel,
        out_shape=jax.ShapeDtypeStruct(gram.shape, jnp.float32),
    )(gram)


def placed_reflector(reflector, first_row, rows_here):
    nb = reflector.shape[0]
    padded = jnp.pad(reflector, ((rows_here - nb, rows_here - nb), (0, 0)))
    return lax.dynamic_slice_in_dim(padded, rows_here - nb - first_row, rows_here, 0)


def shards(eigvecs, reflectors, offsets):
    rows_here = eigvecs.shape[0]
    ticks = reflectors.shape[0]
    gathered = lax.all_gather(reflectors, "vecs", axis=1, tiled=True)
    grams = jnp.einsum("tkr,tks->trs", gathered, gathered, precision=lax.Precision.HIGH, preferred_element_type=jnp.float32)
    solves = tri_inverse(grams)
    first_rows = offsets[:, 0]

    def prepare(step, block):
        reflector = gathered[step]
        solve = solves[step]
        placed = placed_reflector(reflector, first_rows[step], rows_here)
        own_part = lax.optimization_barrier(project_onto(placed[H:], block[: rows_here - H]))
        return placed, own_part, solve

    def finish(block, incoming, placed, own_part, solve):
        project = own_part + project_onto(placed[:H], incoming)
        weights = matmul_3x(solve, project)
        return weights, jnp.concatenate([incoming, block[: rows_here - H]], axis=0)

    def tick(step, carry):
        block, incoming, placed, own_part, solve = carry
        weights, joined = finish(block, incoming, placed, own_part, solve)
        outgoing = block[rows_here - 2 * H : rows_here - H] - matmul_3x(placed[rows_here - H :], weights)
        incoming = passed_along(outgoing, "rows", 1)
        block = joined - matmul_3x(placed, weights)
        return (block, incoming) + prepare(step + 1, block)

    carry = (eigvecs, passed_along(eigvecs[rows_here - H :], "rows", 1)) + prepare(0, eigvecs)
    for step in range(ticks - 1):
        carry = tick(step, carry)
    block, incoming, placed, own_part, solve = carry
    weights, joined = finish(block, incoming, placed, own_part, solve)
    return joined - matmul_3x(placed, weights)


def solution(mesh):
    in_specs = (P("rows", "vecs"), P(None, ("rows", "vecs"), None), P(None, "rows"))
    out_specs = P("rows", "vecs")
    return jax.shard_map(shards, mesh=mesh, in_specs=in_specs, out_specs=out_specs, check_vma=False)
```

```python
import jax
import jax.numpy as jnp
from jax import lax
from jax.experimental import pallas as pl
from jax.sharding import PartitionSpec as P


H = 256
BASE = 32


def passed_along(x, axis, by):
    size = lax.axis_size(axis)
    return lax.ppermute(x, axis, [(i, (i + by) % size) for i in range(size)])


def matmul_3x(left, right):
    return jnp.matmul(left, right, precision=lax.Precision.HIGH, preferred_element_type=jnp.float32)


def project_onto(left, right):
    return lax.dot_general(
        left, right, (((left.ndim - 2,), (right.ndim - 2,)), ((), ())),
        precision=lax.Precision.HIGH, preferred_element_type=jnp.float32,
    )


def half_inverses(blocks, size):
    row = lax.broadcasted_iota(jnp.int32, (size, size), 0)
    col = lax.broadcasted_iota(jnp.int32, (size, size), 1)
    eye_mask = row == col
    eye = eye_mask.astype(jnp.float32)
    same_base = (row // BASE) == (col // BASE)
    diag_cols = [jnp.sum(jnp.where(eye_mask, a, 0.0), axis=1, keepdims=True) for a in blocks]
    diag_rows = [jnp.sum(jnp.where(eye_mask, a, 0.0), axis=0, keepdims=True) for a in blocks]
    powers = [jnp.where(same_base, a / d, 0.0) - eye for a, d in zip(blocks, diag_cols)]
    products = [eye - p for p in powers]
    span = 2
    while span < BASE:
        powers = [matmul_3x(p, p) for p in powers]
        products = [matmul_3x(q, eye + p) for q, p in zip(products, powers)]
        span = span * 2
    invs = [q * (1.0 / d) for q, d in zip(products, diag_rows)]
    half = BASE
    while half < size:
        corner_mask = ((row // half) % 2 == 0) & ((col // half) == (row // half) + 1)
        uppers = [jnp.where(corner_mask, a, 0.0) for a in blocks]
        invs = [v - matmul_3x(matmul_3x(v, u), v) for v, u in zip(invs, uppers)]
        half = half * 2
    return invs


def tri_inverse_kernel(g_ref, o_ref):
    ticks, size = g_ref.shape[0], g_ref.shape[1]
    half = size // 2
    row = lax.broadcasted_iota(jnp.int32, (half, half), 0)
    col = lax.broadcasted_iota(jnp.int32, (half, half), 1)

    def upper_part(x):
        return jnp.where(col > row, x, jnp.where(row == col, x * 0.5, 0.0))

    blocks = []
    for t in range(ticks):
        blocks.append(upper_part(g_ref[t, :half, :half]))
        blocks.append(upper_part(g_ref[t, half:, half:]))
    invs = half_inverses(blocks, half)
    for t in range(ticks):
        upper_inv, lower_inv = invs[2 * t], invs[2 * t + 1]
        corner = -matmul_3x(matmul_3x(upper_inv, g_ref[t, :half, half:]), lower_inv)
        o_ref[t, :half, :half] = upper_inv
        o_ref[t, :half, half:] = corner
        o_ref[t, half:, :half] = jnp.zeros((half, half), jnp.float32)
        o_ref[t, half:, half:] = lower_inv


def tri_inverse(gram):
    return pl.pallas_call(
        tri_inverse_kernel,
        out_shape=jax.ShapeDtypeStruct(gram.shape, jnp.float32),
    )(gram)


def placed_reflector(reflector, first_row, rows_here):
    nb = reflector.shape[0]
    padded = jnp.pad(reflector, ((rows_here - nb, rows_here - nb), (0, 0)))
    return lax.dynamic_slice_in_dim(padded, rows_here - nb - first_row, rows_here, 0)


def shards(eigvecs, reflectors, offsets):
    rows_here = eigvecs.shape[0]
    ticks = reflectors.shape[0]
    gathered = lax.all_gather(reflectors, "vecs", axis=1, tiled=True)
    first_rows = offsets[:, 0]

    def inverse_of(step):
        reflector = gathered[step]
        return tri_inverse(project_onto(reflector, reflector)[None])[0]

    def prepare(step, block):
        placed = placed_reflector(gathered[step], first_rows[step], rows_here)
        own_part = lax.optimization_barrier(project_onto(placed[H:], block[: rows_here - H]))
        return placed, own_part

    def finish(block, incoming, placed, own_part, solve):
        project = own_part + project_onto(placed[:H], incoming)
        weights = matmul_3x(solve, project)
        return weights, jnp.concatenate([incoming, block[: rows_here - H]], axis=0)

    solve = inverse_of(0)
    incoming = passed_along(eigvecs[rows_here - H :], "rows", 1)
    block = eigvecs
    placed, own_part = prepare(0, block)
    for step in range(ticks - 1):
        weights, joined = finish(block, incoming, placed, own_part, solve)
        outgoing = block[rows_here - 2 * H : rows_here - H] - matmul_3x(placed[rows_here - H :], weights)
        incoming = passed_along(outgoing, "rows", 1)
        block = joined - matmul_3x(placed, weights)
        solve = inverse_of(step + 1)
        placed, own_part = prepare(step + 1, block)
    weights, joined = finish(block, incoming, placed, own_part, solve)
    return joined - matmul_3x(placed, weights)


def solution(mesh):
    in_specs = (P("rows", "vecs"), P(None, ("rows", "vecs"), None), P(None, "rows"))
    out_specs = P("rows", "vecs")
    return jax.shard_map(shards, mesh=mesh, in_specs=in_specs, out_specs=out_specs, check_vma=False)
```

```python
import jax
import jax.numpy as jnp
from jax import lax
from jax.experimental import pallas as pl
from jax.sharding import PartitionSpec as P

H = 256
BASE = 32


def passed_along(x, axis, by):
    size = lax.axis_size(axis)
    return lax.ppermute(x, axis, [(i, (i + by) % size) for i in range(size)])


def matmul_3x(left, right):
    return jnp.matmul(left, right, precision=lax.Precision.HIGH, preferred_element_type=jnp.float32)


def project_onto(left, right):
    return lax.dot_general(
        left, right, (((left.ndim - 2,), (right.ndim - 2,)), ((), ())),
        precision=lax.Precision.HIGH, preferred_element_type=jnp.float32,
    )


def half_inverses(blocks, size):
    row = lax.broadcasted_iota(jnp.int32, (size, size), 0)
    col = lax.broadcasted_iota(jnp.int32, (size, size), 1)
    eye_mask = row == col
    eye = eye_mask.astype(jnp.float32)
    same_base = (row // BASE) == (col // BASE)
    diag_cols = [jnp.sum(jnp.where(eye_mask, a, 0.0), axis=1, keepdims=True) for a in blocks]
    diag_rows = [jnp.sum(jnp.where(eye_mask, a, 0.0), axis=0, keepdims=True) for a in blocks]
    powers = [jnp.where(same_base, a / d, 0.0) - eye for a, d in zip(blocks, diag_cols)]
    products = [eye - p for p in powers]
    span = 2
    while span < BASE:
        powers = [matmul_3x(p, p) for p in powers]
        products = [matmul_3x(q, eye + p) for q, p in zip(products, powers)]
        span = span * 2
    invs = [q * (1.0 / d) for q, d in zip(products, diag_rows)]
    half = BASE
    while half < size:
        corner_mask = ((row // half) % 2 == 0) & ((col // half) == (row // half) + 1)
        uppers = [jnp.where(corner_mask, a, 0.0) for a in blocks]
        invs = [v - matmul_3x(matmul_3x(v, u), v) for v, u in zip(invs, uppers)]
        half = half * 2
    return invs


def tri_inverse_kernel(g_ref, o_ref):
    ticks, size = g_ref.shape[0], g_ref.shape[1]
    half = size // 2
    row = lax.broadcasted_iota(jnp.int32, (half, half), 0)
    col = lax.broadcasted_iota(jnp.int32, (half, half), 1)

    def upper_part(x):
        return jnp.where(col > row, x, jnp.where(row == col, x * 0.5, 0.0))

    blocks = []
    for t in range(ticks):
        blocks.append(upper_part(g_ref[t, :half, :half]))
        blocks.append(upper_part(g_ref[t, half:, half:]))
    invs = half_inverses(blocks, half)
    for t in range(ticks):
        upper_inv, lower_inv = invs[2 * t], invs[2 * t + 1]
        corner = -matmul_3x(matmul_3x(upper_inv, g_ref[t, :half, half:]), lower_inv)
        o_ref[t, :half, :half] = upper_inv
        o_ref[t, :half, half:] = corner
        o_ref[t, half:, :half] = jnp.zeros((half, half), jnp.float32)
        o_ref[t, half:, half:] = lower_inv


def tri_inverse(gram):
    return pl.pallas_call(
        tri_inverse_kernel,
        out_shape=jax.ShapeDtypeStruct(gram.shape, jnp.float32),
    )(gram)


def placed_reflector(reflectors, step, first_row, rows_here):
    nb = reflectors.shape[1]
    padded = jnp.pad(reflectors, ((0, 0), (rows_here - nb, rows_here - nb), (0, 0)))
    start = (step, rows_here - nb - first_row, 0)
    return lax.dynamic_slice(padded, start, (1, rows_here, reflectors.shape[2]))[0]


def shards(eigvecs, reflectors, offsets):
    rows_here = eigvecs.shape[0]
    ticks = reflectors.shape[0]
    gathered = lax.all_gather(reflectors, "vecs", axis=1, tiled=True)
    grams = jnp.einsum("tkr,tks->trs", gathered, gathered, precision=lax.Precision.HIGH, preferred_element_type=jnp.float32)
    solves = tri_inverse(grams)
    first_rows = offsets[:, 0]

    def prepare(step, block):
        solve = solves[step]
        placed = placed_reflector(gathered, step, first_rows[step], rows_here)
        own_part = lax.optimization_barrier(project_onto(placed[H:], block[: rows_here - H]))
        return placed, own_part, solve

    def finish(block, incoming, placed, own_part, solve):
        project = own_part + project_onto(placed[:H], incoming)
        weights = matmul_3x(solve, project)
        return weights, jnp.concatenate([incoming, block[: rows_here - H]], axis=0)

    def tick(step, carry):
        block, incoming, placed, own_part, solve = carry
        weights, joined = finish(block, incoming, placed, own_part, solve)
        outgoing = block[rows_here - 2 * H : rows_here - H] - matmul_3x(placed[rows_here - H :], weights)
        incoming = passed_along(outgoing, "rows", 1)
        block = joined - matmul_3x(placed, weights)
        return (block, incoming) + prepare(step + 1, block)

    carry = (eigvecs, passed_along(eigvecs[rows_here - H :], "rows", 1)) + prepare(0, eigvecs)
    for step in range(ticks - 1):
        carry = tick(step, carry)
    block, incoming, placed, own_part, solve = carry
    weights, joined = finish(block, incoming, placed, own_part, solve)
    return joined - matmul_3x(placed, weights)


def solution(mesh):
    in_specs = (P("rows", "vecs"), P(None, ("rows", "vecs"), None), P(None, "rows"))
    out_specs = P("rows", "vecs")
    return jax.shard_map(shards, mesh=mesh, in_specs=in_specs, out_specs=out_specs, check_vma=False)
```

```python
import jax
import jax.numpy as jnp
from jax import lax
from jax.experimental import pallas as pl
from jax.sharding import PartitionSpec as P


H = 256
BASE = 32


def passed_along(x, axis, by):
    size = lax.axis_size(axis)
    return lax.ppermute(x, axis, [(i, (i + by) % size) for i in range(size)])


def matmul_3x(left, right):
    return jnp.matmul(left, right, precision=lax.Precision.HIGH, preferred_element_type=jnp.float32)


def project_onto(left, right):
    return lax.dot_general(
        left, right, (((left.ndim - 2,), (right.ndim - 2,)), ((), ())),
        precision=lax.Precision.HIGH, preferred_element_type=jnp.float32,
    )


def half_inverses(blocks, size):
    row = lax.broadcasted_iota(jnp.int32, (size, size), 0)
    col = lax.broadcasted_iota(jnp.int32, (size, size), 1)
    eye_mask = row == col
    eye = eye_mask.astype(jnp.float32)
    same_base = (row // BASE) == (col // BASE)
    diag_cols = [jnp.sum(jnp.where(eye_mask, a, 0.0), axis=1, keepdims=True) for a in blocks]
    diag_rows = [jnp.sum(jnp.where(eye_mask, a, 0.0), axis=0, keepdims=True) for a in blocks]
    powers = [jnp.where(same_base, a / d, 0.0) - eye for a, d in zip(blocks, diag_cols)]
    products = [eye - p for p in powers]
    span = 2
    while span < BASE:
        powers = [matmul_3x(p, p) for p in powers]
        products = [matmul_3x(q, eye + p) for q, p in zip(products, powers)]
        span = span * 2
    invs = [q * (1.0 / d) for q, d in zip(products, diag_rows)]
    half = BASE
    while half < size:
        corner_mask = ((row // half) % 2 == 0) & ((col // half) == (row // half) + 1)
        uppers = [jnp.where(corner_mask, a, 0.0) for a in blocks]
        invs = [v - matmul_3x(matmul_3x(v, u), v) for v, u in zip(invs, uppers)]
        half = half * 2
    return invs


def tri_inverse_kernel(g_ref, o_ref):
    ticks, size = g_ref.shape[0], g_ref.shape[1]
    half = size // 2
    row = lax.broadcasted_iota(jnp.int32, (half, half), 0)
    col = lax.broadcasted_iota(jnp.int32, (half, half), 1)

    def upper_part(x):
        return jnp.where(col > row, x, jnp.where(row == col, x * 0.5, 0.0))

    blocks = []
    for t in range(ticks):
        blocks.append(upper_part(g_ref[t, :half, :half]))
        blocks.append(upper_part(g_ref[t, half:, half:]))
    invs = half_inverses(blocks, half)
    for t in range(ticks):
        upper_inv, lower_inv = invs[2 * t], invs[2 * t + 1]
        corner = -matmul_3x(matmul_3x(upper_inv, g_ref[t, :half, half:]), lower_inv)
        o_ref[t, :half, :half] = upper_inv
        o_ref[t, :half, half:] = corner
        o_ref[t, half:, :half] = jnp.zeros((half, half), jnp.float32)
        o_ref[t, half:, half:] = lower_inv


def tri_inverse(gram):
    return pl.pallas_call(
        tri_inverse_kernel,
        out_shape=jax.ShapeDtypeStruct(gram.shape, jnp.float32),
    )(gram)


def placed_reflector(reflectors, step, first_row, rows_here):
    nb = reflectors.shape[1]
    padded = jnp.pad(reflectors, ((0, 0), (rows_here - nb, rows_here - nb), (0, 0)))
    start = (step, rows_here - nb - first_row, 0)
    return lax.dynamic_slice(padded, start, (1, rows_here, reflectors.shape[2]))[0]


def shards(eigvecs, reflectors, offsets):
    rows_here = eigvecs.shape[0]
    ticks = reflectors.shape[0]
    gathered = lax.all_gather(reflectors, "vecs", axis=1, tiled=True)
    first = gathered[0]
    solves = [tri_inverse(project_onto(first, first)[None])[0]]
    first_rows = offsets[:, 0]

    def prepare(step, block):
        solve = solves[step]
        placed = placed_reflector(gathered, step, first_rows[step], rows_here)
        own_part = lax.optimization_barrier(project_onto(placed[H:], block[: rows_here - H]))
        return placed, own_part, solve

    def finish(block, incoming, placed, own_part, solve):
        project = own_part + project_onto(placed[:H], incoming)
        weights = matmul_3x(solve, project)
        return weights, jnp.concatenate([incoming, block[: rows_here - H]], axis=0)

    def tick(step, carry):
        block, incoming, placed, own_part, solve = carry
        weights, joined = finish(block, incoming, placed, own_part, solve)
        outgoing = block[rows_here - 2 * H : rows_here - H] - matmul_3x(placed[rows_here - H :], weights)
        incoming = passed_along(outgoing, "rows", 1)
        block = joined - matmul_3x(placed, weights)
        if step == 0:
            rest = gathered[1:]
            grams = jnp.einsum("tkr,tks->trs", rest, rest, precision=lax.Precision.HIGH, preferred_element_type=jnp.float32)
            later = tri_inverse(grams)
            solves.extend(later[i] for i in range(later.shape[0]))
        prepared = prepare(step + 1, block)
        return (block, incoming) + prepared

    carry = (eigvecs, passed_along(eigvecs[rows_here - H :], "rows", 1)) + prepare(0, eigvecs)
    for step in range(ticks - 1):
        carry = tick(step, carry)
    block, incoming, placed, own_part, solve = carry
    weights, joined = finish(block, incoming, placed, own_part, solve)
    return joined - matmul_3x(placed, weights)


def solution(mesh):
    in_specs = (P("rows", "vecs"), P(None, ("rows", "vecs"), None), P(None, "rows"))
    out_specs = P("rows", "vecs")
    return jax.shard_map(shards, mesh=mesh, in_specs=in_specs, out_specs=out_specs, check_vma=False)
```

```python
import jax
import jax.numpy as jnp
from jax import lax
from jax.experimental import pallas as pl
from jax.experimental.pallas import tpu as pltpu
from jax.sharding import PartitionSpec as P

H = 256
BASE = 32


def passed_along(x, axis, by):
    size = lax.axis_size(axis)
    return lax.ppermute(x, axis, [(i, (i + by) % size) for i in range(size)])


def matmul_3x(left, right):
    return jnp.matmul(left, right, precision=lax.Precision.HIGH, preferred_element_type=jnp.float32)


def project_onto(left, right):
    return lax.dot_general(
        left, right, (((left.ndim - 2,), (right.ndim - 2,)), ((), ())),
        precision=lax.Precision.HIGH, preferred_element_type=jnp.float32,
    )


def half_inverses(blocks, size):
    row = lax.broadcasted_iota(jnp.int32, (size, size), 0)
    col = lax.broadcasted_iota(jnp.int32, (size, size), 1)
    eye_mask = row == col
    eye = eye_mask.astype(jnp.float32)
    same_base = (row // BASE) == (col // BASE)
    diag_cols = [jnp.sum(jnp.where(eye_mask, a, 0.0), axis=1, keepdims=True) for a in blocks]
    diag_rows = [jnp.sum(jnp.where(eye_mask, a, 0.0), axis=0, keepdims=True) for a in blocks]
    powers = [jnp.where(same_base, a / d, 0.0) - eye for a, d in zip(blocks, diag_cols)]
    products = [eye - p for p in powers]
    span = 2
    while span < BASE:
        powers = [matmul_3x(p, p) for p in powers]
        products = [matmul_3x(q, eye + p) for q, p in zip(products, powers)]
        span = span * 2
    invs = [q * (1.0 / d) for q, d in zip(products, diag_rows)]
    half = BASE
    while half < size:
        corner_mask = ((row // half) % 2 == 0) & ((col // half) == (row // half) + 1)
        uppers = [jnp.where(corner_mask, a, 0.0) for a in blocks]
        invs = [v - matmul_3x(matmul_3x(v, u), v) for v, u in zip(invs, uppers)]
        half = half * 2
    return invs


def tri_inverse_kernel(v_ref, o_ref):
    ticks, size = v_ref.shape[0], v_ref.shape[2]
    half = size // 2
    row = lax.broadcasted_iota(jnp.int32, (half, half), 0)
    col = lax.broadcasted_iota(jnp.int32, (half, half), 1)

    def upper_part(x):
        return jnp.where(col > row, x, jnp.where(row == col, x * 0.5, 0.0))

    grams = []
    for t in range(ticks):
        v = v_ref[t]
        grams.append(lax.dot_general(
            v, v, (((0,), (0,)), ((), ())),
            precision=lax.Precision.HIGH, preferred_element_type=jnp.float32,
        ))
    blocks = []
    for g in grams:
        blocks.append(upper_part(g[:half, :half]))
        blocks.append(upper_part(g[half:, half:]))
    invs = half_inverses(blocks, half)
    for t in range(ticks):
        upper_inv, lower_inv = invs[2 * t], invs[2 * t + 1]
        corner = -matmul_3x(matmul_3x(upper_inv, grams[t][:half, half:]), lower_inv)
        o_ref[t, :half, :half] = upper_inv
        o_ref[t, :half, half:] = corner
        o_ref[t, half:, :half] = jnp.zeros((half, half), jnp.float32)
        o_ref[t, half:, half:] = lower_inv


def tri_inverse(reflectors):
    ticks, kb = reflectors.shape[0], reflectors.shape[2]
    return pl.pallas_call(
        tri_inverse_kernel,
        out_shape=jax.ShapeDtypeStruct((ticks, kb, kb), jnp.float32),
        compiler_params=pltpu.CompilerParams(vmem_limit_bytes=48 * 1024 * 1024),
    )(reflectors)


def placed_reflector(reflectors, step, first_row, rows_here):
    nb = reflectors.shape[1]
    padded = jnp.pad(reflectors, ((0, 0), (rows_here - nb, rows_here - nb), (0, 0)))
    start = (step, rows_here - nb - first_row, 0)
    return lax.dynamic_slice(padded, start, (1, rows_here, reflectors.shape[2]))[0]


def shards(eigvecs, reflectors, offsets):
    rows_here = eigvecs.shape[0]
    ticks = reflectors.shape[0]
    gathered = lax.all_gather(reflectors, "vecs", axis=1, tiled=True)
    solves = tri_inverse(gathered)
    first_rows = offsets[:, 0]

    def prepare(step, block):
        solve = solves[step]
        placed = placed_reflector(gathered, step, first_rows[step], rows_here)
        own_part = lax.optimization_barrier(project_onto(placed[H:], block[: rows_here - H]))
        return placed, own_part, solve

    def finish(block, incoming, placed, own_part, solve):
        project = own_part + project_onto(placed[:H], incoming)
        weights = matmul_3x(solve, project)
        return weights, jnp.concatenate([incoming, block[: rows_here - H]], axis=0)

    def tick(step, carry):
        block, incoming, placed, own_part, solve = carry
        weights, joined = finish(block, incoming, placed, own_part, solve)
        outgoing = block[rows_here - 2 * H : rows_here - H] - matmul_3x(placed[rows_here - H :], weights)
        incoming = passed_along(outgoing, "rows", 1)
        block = joined - matmul_3x(placed, weights)
        return (block, incoming) + prepare(step + 1, block)

    carry = (eigvecs, passed_along(eigvecs[rows_here - H :], "rows", 1)) + prepare(0, eigvecs)
    for step in range(ticks - 1):
        carry = tick(step, carry)
    block, incoming, placed, own_part, solve = carry
    weights, joined = finish(block, incoming, placed, own_part, solve)
    return joined - matmul_3x(placed, weights)


def solution(mesh):
    in_specs = (P("rows", "vecs"), P(None, ("rows", "vecs"), None), P(None, "rows"))
    out_specs = P("rows", "vecs")
    return jax.shard_map(shards, mesh=mesh, in_specs=in_specs, out_specs=out_specs, check_vma=False)
```
